256 devices in a mesh: bz: 16 (over x_hi, y, core), bxy: 16 (over z, x_lo).
Axes of the slice: x: 4 (x_hi: 2, x_lo: 2; x = x_hi * 2 + x_lo), y: 4, z: 8, core: 2. Of those that a mesh axis runs over, the one named last changes fastest.
Arguments:
- estimate: float32 [128, 256, 512], P('bz', 'bxy'), may hold values from 0.5 to 2
- observed: bfloat16 [3, 128, 256, 512], P(None, 'bz', 'bxy'), may hold values from 0.5 to 2
- psf_taps: float32 [3, 3, 3, 9], replicated, may hold values from 0.05 to 1
- view_shift: int32 [3], replicated, may hold values from 0 to 511
- intersection: int32 [3, 16, 16], replicated, may hold values 0 or 1
Outputs:
- updated: float32 [128, 256, 512], P('bz', 'bxy')
The draws below stay inside these ranges and needn't reach their ends.
All inputs are finite; a program needn't handle non-finite values.
Results may differ from the reference program's by a relative error of at most 0.0004.
Values may be sent and summed in bfloat16 or wider, within the bound.
No kernel may reach another device: no remote copies, remote signals or barrier semaphores. Data moves between devices by JAX's collectives and lax.ppermute only.
A program may use at most 64 MiB of HBM per device.

```python
import math
import jax
import jax.numpy as jnp
from jax import lax

CZ = 8
CX = 16
NY = 512
VIEWS = 3
RANK = 3
RADIUS = 4
PASSES = 8
TAPS = 9
NZ = 128
NX = 256
BRICKS_Z = 16
BRICKS_X = 16


def touch_ends(array, key, smallest, largest):
    spot = [jax.random.randint(jax.random.fold_in(key, axis), (), 0, length) for axis, length in enumerate(array.shape)]
    widest = array.shape.index(max(array.shape))
    neighbour = spot[:widest] + [(spot[widest] + 1) % array.shape[widest]] + spot[widest + 1:]
    return array.at[tuple(spot)].set(smallest).at[tuple(neighbour)].set(largest)


def steps_of(stream_key, extent, shards, least, largest):
    factor_of = 1.0
    for axis_at, parts in shards:
        heights = jax.random.uniform(jax.random.fold_in(jax.random.fold_in(stream_key, 6), axis_at), (parts,), jnp.float32, least / len(shards), largest / len(shards))
        factor_of = factor_of * jnp.repeat(jnp.exp(heights), extent[axis_at] // parts).reshape((-1,) + (1,) * (len(extent) - 1 - axis_at))
    return factor_of


def setup_inputs(seed: int = 0) -> dict:
    key_of = jax.random.split(jax.random.key(seed), 6)
    estimate = jnp.clip(0.5 + 1.5 * jax.random.uniform(key_of[0], (NZ, NX, NY), jnp.float32) ** steps_of(key_of[0], (NZ, NX, NY), ((0, 16), (1, 16)), -0.2, 0.2), 0.5, 2.0)
    observed = jnp.clip(0.5 + 1.5 * jax.random.uniform(key_of[1], (VIEWS, NZ, NX, NY), jnp.float32) ** steps_of(key_of[1], (VIEWS, NZ, NX, NY), ((1, 16), (2, 16)), -0.2, 0.2), 0.5, 2.0).astype(jnp.bfloat16)
    psf_taps = jnp.clip(jnp.exp(jax.random.uniform(key_of[2], (VIEWS, RANK, 3, TAPS), jnp.float32, math.log(0.05), math.log(1.0))), 0.05, 1.0)
    view_shift = jax.random.randint(key_of[3], (VIEWS,), 0, NY).astype(jnp.int32)
    intersection = touch_ends((jax.random.randint(key_of[4], (VIEWS, BRICKS_Z, BRICKS_X), 0, 4) < 3).astype(jnp.int32), jax.random.fold_in(key_of[4], 1), 0, 1)
    return {"estimate": estimate, "observed": observed, "psf_taps": psf_taps, "view_shift": view_shift, "intersection": intersection}


EPS_TV = 0.25
TAU = 0.08
BACKGROUND = 0.1

def tv_pass(field):
    padded = jnp.pad(field, 1, mode='edge')
    beside_list = (padded[:-2, 1:-1, 1:-1], padded[2:, 1:-1, 1:-1], padded[1:-1, :-2, 1:-1], padded[1:-1, 2:, 1:-1], padded[1:-1, 1:-1, :-2], padded[1:-1, 1:-1, 2:])
    total = jnp.zeros_like(field)
    for beside in beside_list:
        diff = beside - field
        total = total + diff / jnp.sqrt(diff * diff + EPS_TV)
    return field + TAU * total

def conv_valid(values, kernel, axis):
    length = values.shape[axis] - (kernel.shape[0] - 1)
    total = kernel[0] * lax.slice_in_dim(values, 0, length, axis=axis)
    for tap in range(1, kernel.shape[0]):
        total = total + kernel[tap] * lax.slice_in_dim(values, tap, tap + length, axis=axis)
    return total

def conv_full(values, kernel, axis):
    widths = [(0, 0)] * 3
    widths[axis] = (RADIUS, RADIUS)
    return conv_valid(jnp.pad(values, widths), kernel, axis)

def reference(estimate, observed, psf_taps, view_shift, intersection):
    smoothed = estimate
    for pass_index in range(PASSES):
        smoothed = tv_pass(smoothed)
    sent = lax.optimization_barrier(smoothed.astype(jnp.bfloat16))
    sent_full = sent.astype(jnp.float32)
    kernels = psf_taps / lax.optimization_barrier(jnp.sum(psf_taps, axis=-1, keepdims=True))
    cell_mask = jnp.repeat(jnp.repeat(intersection, CZ, axis=1), CX, axis=2)
    correction = jnp.zeros(estimate.shape, jnp.float32)
    for view in range(VIEWS):
        moved = jnp.roll(sent_full, view_shift[view], axis=2)
        image = jnp.zeros(estimate.shape, jnp.float32)
        for rank_index in range(RANK):
            blurred = conv_full(moved, kernels[view, rank_index, 2], 2)
            blurred = conv_full(blurred, kernels[view, rank_index, 1], 1)
            blurred = conv_full(blurred, kernels[view, rank_index, 0], 0)
            image = image + blurred
        image = image / RANK
        ratio = jnp.where(cell_mask[view][:, :, None] > 0, observed[view].astype(jnp.float32) / (image + BACKGROUND), 1.0)
        ratio = lax.optimization_barrier(ratio.astype(jnp.bfloat16)).astype(jnp.float32)
        back = jnp.zeros(estimate.shape, jnp.float32)
        for rank_index in range(RANK):
            spread = conv_full(ratio, kernels[view, rank_index, 0][::-1], 0)
            spread = conv_full(spread, kernels[view, rank_index, 1][::-1], 1)
            spread = conv_full(spread, kernels[view, rank_index, 2][::-1], 2)
            back = back + spread
        back = back / RANK
        correction = correction + jnp.roll(back, -view_shift[view], axis=2)
    return smoothed * correction / VIEWS
```

```python
import jax
import jax.numpy as jnp
from jax import lax
from jax.sharding import PartitionSpec as P

VIEWS = 3
RANK = 3
RADIUS = 4
PASSES = 8


EPS_TV = 0.25
TAU = 0.08
BACKGROUND = 0.1
HIGHEST = lax.Precision.HIGHEST


def extended(cells, sides, width):
    for axis, dim in sides:
        count = lax.axis_size(axis)
        ends = count - 1
        head = lax.slice_in_dim(cells, 0, width, axis=dim)
        tail = lax.slice_in_dim(cells, cells.shape[dim] - width, cells.shape[dim], axis=dim)
        cells = jnp.concatenate(
            [
                lax.ppermute(tail, axis, [(i, (i + 1) % count) for i in range(ends)]),
                cells,
                lax.ppermute(head, axis, [((i + 1) % count, i) for i in range(ends)]),
            ],
            axis=dim,
        )
    return cells


def tv_pass(padded, z_first, x_first, cells_z, cells_x):
    rows_z = padded.shape[0] - 2
    rows_x = padded.shape[1] - 2
    field = padded[1:-1, 1:-1]
    zcoords = z_first + lax.iota(jnp.int32, rows_z + 2)
    xcoords = x_first + lax.iota(jnp.int32, rows_x + 2)
    z_inside = ((zcoords >= 0) & (zcoords < cells_z))[:, None, None]
    x_inside = ((xcoords >= 0) & (xcoords < cells_x))[None, :, None]
    y_lower = jnp.concatenate([field[:, :, :1], field[:, :, :-1]], axis=2)
    y_upper = jnp.concatenate([field[:, :, 1:], field[:, :, -1:]], axis=2)
    pairs = (
        (padded[:-2, 1:-1], z_inside[:-2]),
        (padded[2:, 1:-1], z_inside[2:]),
        (padded[1:-1, :-2], x_inside[:, :-2]),
        (padded[1:-1, 2:], x_inside[:, 2:]),
        (y_lower, True),
        (y_upper, True),
    )
    total = jnp.zeros_like(field)
    for beside, inside in pairs:
        diff = beside - field
        total = total + jnp.where(inside, diff / jnp.sqrt(diff * diff + EPS_TV), 0.0)
    return field + TAU * total


def band(taps, rows, cols):
    gap = lax.iota(jnp.int32, cols)[None, :] - lax.iota(jnp.int32, rows)[:, None]
    out = jnp.zeros(taps.shape[:-1] + (rows, cols), jnp.float32)
    for tap in range(taps.shape[-1]):
        out = out + jnp.where(gap == tap, taps[..., tap, None, None], 0.0)
    return out


def plane_matrices(kz, kx, cz, cx):
    wz = band(kz, cz, cz + 2 * RADIUS)
    wx = band(kx, cx, cx + 2 * RADIUS)
    w = wz[..., :, None, :, None] * wx[..., None, :, None, :]
    lead = w.shape[:-4]
    return w.reshape(lead + (cz * cx, (cz + 2 * RADIUS) * (cx + 2 * RADIUS)))


def line_matrices(ky, shift, ny):
    rows = lax.iota(jnp.int32, ny)[None, :, None] + shift[:, None, None]
    rows = jnp.where(rows >= ny, rows - ny, rows)
    gap = rows - lax.iota(jnp.int32, ny)[None, None, :] + RADIUS
    gap = gap[:, None]
    out = jnp.zeros(ky.shape[:-1] + (ny, ny), jnp.float32)
    for tap in range(ky.shape[-1]):
        out = out + jnp.where(gap == tap, ky[..., tap, None, None], 0.0)
    return out


def local(estimate, observed, psf_taps, view_shift, intersection):
    cz_here, cx_here, cells_y = estimate.shape
    bricks_z = lax.axis_size("bz")
    bricks_x = lax.axis_size("bxy")
    cells_z = cz_here * bricks_z
    cells_x = cx_here * bricks_x
    brick_z = lax.axis_index("bz")
    brick_x = lax.axis_index("bxy")
    z_base = brick_z * cz_here
    x_base = brick_x * cx_here
    smoothed = extended(estimate, (("bz", 0), ("bxy", 1)), PASSES)
    for pass_index in range(PASSES):
        reach = PASSES - pass_index
        smoothed = tv_pass(smoothed, z_base - reach, x_base - reach, cells_z, cells_x)
    sent = smoothed.astype(jnp.bfloat16)
    sent_pad = extended(sent, (("bz", 0), ("bxy", 1)), RADIUS)
    rows_pad = (cz_here + 2 * RADIUS) * (cx_here + 2 * RADIUS)
    rows = cz_here * cx_here
    sent_flat = sent_pad.astype(jnp.float32).reshape(rows_pad, cells_y)
    kernels = psf_taps / jnp.sum(psf_taps, axis=-1, keepdims=True)
    fwd_plane = plane_matrices(kernels[:, :, 0], kernels[:, :, 1], cz_here, cx_here)
    adj_plane = plane_matrices(kernels[:, :, 0, ::-1], kernels[:, :, 1, ::-1], cz_here, cx_here)
    lines = line_matrices(kernels[:, :, 2], view_shift, cells_y)
    planes = jnp.einsum("vrqp,pj->vrqj", fwd_plane, sent_flat, precision=HIGHEST)
    images = jnp.einsum("vrqi,vrij->vqj", planes, lines, precision=HIGHEST) / RANK
    images = images.reshape(VIEWS, cz_here, cx_here, cells_y)
    flags = intersection[:, brick_z, brick_x]
    ratios = jnp.where(
        flags[:, None, None, None] > 0,
        observed.astype(jnp.float32) / (images + BACKGROUND),
        1.0,
    ).astype(jnp.bfloat16)
    ratio_pad = extended(ratios, (("bz", 1), ("bxy", 2)), RADIUS)
    ratio_flat = ratio_pad.astype(jnp.float32).reshape(VIEWS, rows_pad, cells_y)
    spread = jnp.einsum("vrqp,vpj->vrqj", adj_plane, ratio_flat, precision=HIGHEST)
    correction = jnp.einsum("vrqi,vrji->qj", spread, lines, precision=HIGHEST) / RANK
    correction = correction.reshape(cz_here, cx_here, cells_y)
    return smoothed * correction / VIEWS


def solution(mesh):
    return jax.shard_map(
        local,
        mesh=mesh,
        in_specs=(P("bz", "bxy", None), P(None, "bz", "bxy", None), P(), P(), P()),
        out_specs=P("bz", "bxy", None),
        check_vma=False,
    )
```

```python
import jax
import jax.numpy as jnp
from jax import lax
from jax.sharding import PartitionSpec as P

VIEWS = 3
RANK = 3
RADIUS = 4
PASSES = 8


EPS_TV = 0.25
TAU = 0.08
BACKGROUND = 0.1
HIGHEST = lax.Precision.HIGHEST
HIGH = lax.Precision.HIGH


def extended(cells, sides, width):
    (axis_z, dim_z), (axis_x, dim_x) = sides
    count_z = lax.axis_size(axis_z)
    count_x = lax.axis_size(axis_x)
    both = (axis_z, axis_x)

    def part(block, dz, dx):
        pairs = []
        for iz in range(count_z):
            for ix in range(count_x):
                tz, tx = iz + dz, ix + dx
                if 0 <= tz < count_z and 0 <= tx < count_x:
                    pairs.append((iz * count_x + ix, tz * count_x + tx))
        if dz == 0:
            return lax.ppermute(block, axis_x, [(i, i + dx) for i in range(count_x) if 0 <= i + dx < count_x])
        if dx == 0:
            return lax.ppermute(block, axis_z, [(i, i + dz) for i in range(count_z) if 0 <= i + dz < count_z])
        return lax.ppermute(block, both, pairs)

    size_z = cells.shape[dim_z]
    size_x = cells.shape[dim_x]
    head_z = lax.slice_in_dim(cells, 0, width, axis=dim_z)
    tail_z = lax.slice_in_dim(cells, size_z - width, size_z, axis=dim_z)
    pieces = []
    for dz, rows in ((1, tail_z), (0, cells), (-1, head_z)):
        head_x = lax.slice_in_dim(rows, 0, width, axis=dim_x)
        tail_x = lax.slice_in_dim(rows, size_x - width, size_x, axis=dim_x)
        line = []
        for dx, block in ((1, tail_x), (0, rows), (-1, head_x)):
            line.append(block if dz == 0 and dx == 0 else part(block, dz, dx))
        pieces.append(jnp.concatenate(line, axis=dim_x))
    return jnp.concatenate(pieces, axis=dim_z)


def tv_pass(padded, z_first, x_first, cells_z, cells_x):
    rows_z = padded.shape[0] - 2
    rows_x = padded.shape[1] - 2
    field = padded[1:-1, 1:-1]
    zcoords = z_first + lax.iota(jnp.int32, rows_z + 2)
    xcoords = x_first + lax.iota(jnp.int32, rows_x + 2)
    z_inside = ((zcoords >= 0) & (zcoords < cells_z))[:, None, None]
    x_inside = ((xcoords >= 0) & (xcoords < cells_x))[None, :, None]
    y_lower = jnp.concatenate([field[:, :, :1], field[:, :, :-1]], axis=2)
    y_upper = jnp.concatenate([field[:, :, 1:], field[:, :, -1:]], axis=2)
    pairs = (
        (padded[:-2, 1:-1], z_inside[:-2]),
        (padded[2:, 1:-1], z_inside[2:]),
        (padded[1:-1, :-2], x_inside[:, :-2]),
        (padded[1:-1, 2:], x_inside[:, 2:]),
        (y_lower, True),
        (y_upper, True),
    )
    total = jnp.zeros_like(field)
    for beside, inside in pairs:
        diff = beside - field
        total = total + jnp.where(inside, diff / jnp.sqrt(diff * diff + EPS_TV), 0.0)
    return field + TAU * total


def band(taps, rows, cols):
    gap = lax.iota(jnp.int32, cols)[None, :] - lax.iota(jnp.int32, rows)[:, None]
    out = jnp.zeros(taps.shape[:-1] + (rows, cols), jnp.float32)
    for tap in range(taps.shape[-1]):
        out = out + jnp.where(gap == tap, taps[..., tap, None, None], 0.0)
    return out


def plane_matrices(kz, kx, cz, cx):
    wz = band(kz, cz, cz + 2 * RADIUS)
    wx = band(kx, cx, cx + 2 * RADIUS)
    wide = cx + 2 * RADIUS
    q = lax.iota(jnp.int32, cz * cx)
    p = lax.iota(jnp.int32, (cz + 2 * RADIUS) * wide)
    pick_qz = (q[:, None] // cx == lax.iota(jnp.int32, cz)[None, :]).astype(jnp.float32)
    pick_qx = (q[:, None] % cx == lax.iota(jnp.int32, cx)[None, :]).astype(jnp.float32)
    pick_pz = (lax.iota(jnp.int32, cz + 2 * RADIUS)[:, None] == p[None, :] // wide).astype(jnp.float32)
    pick_px = (lax.iota(jnp.int32, wide)[:, None] == p[None, :] % wide).astype(jnp.float32)
    full_z = jnp.einsum("qa,...ab,bp->...qp", pick_qz, wz, pick_pz, precision=HIGHEST)
    full_x = jnp.einsum("qa,...ab,bp->...qp", pick_qx, wx, pick_px, precision=HIGHEST)
    return full_z * full_x


def line_matrices(ky, shift, ny):
    rows = lax.iota(jnp.int32, ny)[None, :, None] + shift[:, None, None]
    rows = jnp.where(rows >= ny, rows - ny, rows)
    gap = rows - lax.iota(jnp.int32, ny)[None, None, :] + RADIUS
    gap = gap[:, None]
    out = jnp.zeros(ky.shape[:-1] + (ny, ny), jnp.float32)
    for tap in range(ky.shape[-1]):
        out = out + jnp.where(gap == tap, ky[..., tap, None, None], 0.0)
    return out


def local(estimate, observed, psf_taps, view_shift, intersection):
    cz_here, cx_here, cells_y = estimate.shape
    bricks_z = lax.axis_size("bz")
    bricks_x = lax.axis_size("bxy")
    cells_z = cz_here * bricks_z
    cells_x = cx_here * bricks_x
    brick_z = lax.axis_index("bz")
    brick_x = lax.axis_index("bxy")
    z_base = brick_z * cz_here
    x_base = brick_x * cx_here
    smoothed = extended(estimate, (("bz", 0), ("bxy", 1)), PASSES)
    for pass_index in range(PASSES):
        reach = PASSES - pass_index
        smoothed = tv_pass(smoothed, z_base - reach, x_base - reach, cells_z, cells_x)
    sent = smoothed.astype(jnp.bfloat16)
    sent_pad = extended(sent, (("bz", 0), ("bxy", 1)), RADIUS)
    rows_pad = (cz_here + 2 * RADIUS) * (cx_here + 2 * RADIUS)
    rows = cz_here * cx_here
    sent_flat = sent_pad.astype(jnp.float32).reshape(rows_pad, cells_y)
    kernels = psf_taps / jnp.sum(psf_taps, axis=-1, keepdims=True)
    fwd_plane = plane_matrices(kernels[:, :, 0], kernels[:, :, 1], cz_here, cx_here)
    adj_plane = plane_matrices(kernels[:, :, 0, ::-1], kernels[:, :, 1, ::-1], cz_here, cx_here)
    lines = lax.optimization_barrier(line_matrices(kernels[:, :, 2], view_shift, cells_y))
    planes = jnp.einsum("vrqp,pj->vrqj", fwd_plane, sent_flat, precision=HIGH)
    images = jnp.einsum("vrqi,vrij->vqj", planes, lines, precision=HIGH) / RANK
    images = images.reshape(VIEWS, cz_here, cx_here, cells_y)
    flags = intersection[:, brick_z, brick_x]
    ratios = jnp.where(
        flags[:, None, None, None] > 0,
        observed.astype(jnp.float32) / (images + BACKGROUND),
        1.0,
    ).astype(jnp.bfloat16)
    ratio_pad = extended(ratios, (("bz", 1), ("bxy", 2)), RADIUS)
    ratio_flat = ratio_pad.astype(jnp.float32).reshape(VIEWS, rows_pad, cells_y)
    spread = jnp.einsum("vrqp,vpj->vrqj", adj_plane, ratio_flat, precision=HIGH)
    correction = jnp.einsum("vrqi,vrji->qj", spread, lines, precision=HIGH) / RANK
    correction = correction.reshape(cz_here, cx_here, cells_y)
    return smoothed * correction / VIEWS


def solution(mesh):
    return jax.shard_map(
        local,
        mesh=mesh,
        in_specs=(P("bz", "bxy", None), P(None, "bz", "bxy", None), P(), P(), P()),
        out_specs=P("bz", "bxy", None),
        check_vma=False,
    )
```

```python
import jax
import jax.numpy as jnp
from jax import lax
from jax.sharding import PartitionSpec as P

VIEWS = 3
RANK = 3
RADIUS = 4
PASSES = 8


EPS_TV = 0.25
TAU = 0.08
BACKGROUND = 0.1
HIGHEST = lax.Precision.HIGHEST
HIGH = lax.Precision.HIGH


def extended(cells, sides, width):
    for axis, dim in sides:
        count = lax.axis_size(axis)
        ends = count - 1
        head = lax.slice_in_dim(cells, 0, width, axis=dim)
        tail = lax.slice_in_dim(cells, cells.shape[dim] - width, cells.shape[dim], axis=dim)
        cells = jnp.concatenate(
            [
                lax.ppermute(tail, axis, [(i, (i + 1) % count) for i in range(ends)]),
                cells,
                lax.ppermute(head, axis, [((i + 1) % count, i) for i in range(ends)]),
            ],
            axis=dim,
        )
    return cells


def tv_pass(padded, z_first, x_first, cells_z, cells_x):
    rows_z = padded.shape[0] - 2
    rows_x = padded.shape[1] - 2
    field = padded[1:-1, 1:-1]
    zcoords = z_first + lax.iota(jnp.int32, rows_z + 2)
    xcoords = x_first + lax.iota(jnp.int32, rows_x + 2)
    z_inside = ((zcoords >= 0) & (zcoords < cells_z))[:, None, None]
    x_inside = ((xcoords >= 0) & (xcoords < cells_x))[None, :, None]
    y_lower = jnp.concatenate([field[:, :, :1], field[:, :, :-1]], axis=2)
    y_upper = jnp.concatenate([field[:, :, 1:], field[:, :, -1:]], axis=2)
    pairs = (
        (padded[:-2, 1:-1], z_inside[:-2]),
        (padded[2:, 1:-1], z_inside[2:]),
        (padded[1:-1, :-2], x_inside[:, :-2]),
        (padded[1:-1, 2:], x_inside[:, 2:]),
        (y_lower, True),
        (y_upper, True),
    )
    total = jnp.zeros_like(field)
    for beside, inside in pairs:
        diff = beside - field
        total = total + jnp.where(inside, diff / jnp.sqrt(diff * diff + EPS_TV), 0.0)
    return field + TAU * total


def band(taps, rows, cols):
    gap = lax.iota(jnp.int32, cols)[None, :] - lax.iota(jnp.int32, rows)[:, None]
    out = jnp.zeros(taps.shape[:-1] + (rows, cols), jnp.float32)
    for tap in range(taps.shape[-1]):
        out = out + jnp.where(gap == tap, taps[..., tap, None, None], 0.0)
    return out


def plane_matrices(kz, kx, cz, cx):
    wz = band(kz, cz, cz + 2 * RADIUS)
    wx = band(kx, cx, cx + 2 * RADIUS)
    wide = cx + 2 * RADIUS
    q = lax.iota(jnp.int32, cz * cx)
    p = lax.iota(jnp.int32, (cz + 2 * RADIUS) * wide)
    pick_qz = (q[:, None] // cx == lax.iota(jnp.int32, cz)[None, :]).astype(jnp.float32)
    pick_qx = (q[:, None] % cx == lax.iota(jnp.int32, cx)[None, :]).astype(jnp.float32)
    pick_pz = (lax.iota(jnp.int32, cz + 2 * RADIUS)[:, None] == p[None, :] // wide).astype(jnp.float32)
    pick_px = (lax.iota(jnp.int32, wide)[:, None] == p[None, :] % wide).astype(jnp.float32)
    full_z = jnp.einsum("qa,...ab,bp->...qp", pick_qz, wz, pick_pz, precision=HIGHEST)
    full_x = jnp.einsum("qa,...ab,bp->...qp", pick_qx, wx, pick_px, precision=HIGHEST)
    return full_z * full_x


def line_matrices(ky, shift, ny):
    rows = lax.iota(jnp.int32, ny)[None, :, None] + shift[:, None, None]
    rows = jnp.where(rows >= ny, rows - ny, rows)
    gap = rows - lax.iota(jnp.int32, ny)[None, None, :] + RADIUS
    gap = gap[:, None]
    out = jnp.zeros(ky.shape[:-1] + (ny, ny), jnp.float32)
    for tap in range(ky.shape[-1]):
        out = out + jnp.where(gap == tap, ky[..., tap, None, None], 0.0)
    return out


def local(estimate, observed, psf_taps, view_shift, intersection):
    cz_here, cx_here, cells_y = estimate.shape
    bricks_z = lax.axis_size("bz")
    bricks_x = lax.axis_size("bxy")
    cells_z = cz_here * bricks_z
    cells_x = cx_here * bricks_x
    brick_z = lax.axis_index("bz")
    brick_x = lax.axis_index("bxy")
    z_base = brick_z * cz_here
    x_base = brick_x * cx_here
    smoothed = extended(estimate, (("bz", 0), ("bxy", 1)), PASSES)
    for pass_index in range(PASSES):
        reach = PASSES - pass_index
        smoothed = tv_pass(smoothed, z_base - reach, x_base - reach, cells_z, cells_x)
    sent = smoothed.astype(jnp.bfloat16)
    sent_pad = extended(sent, (("bz", 0), ("bxy", 1)), RADIUS)
    rows_pad = (cz_here + 2 * RADIUS) * (cx_here + 2 * RADIUS)
    rows = cz_here * cx_here
    sent_flat = sent_pad.astype(jnp.float32).reshape(rows_pad, cells_y)
    kernels = psf_taps / jnp.sum(psf_taps, axis=-1, keepdims=True)
    fwd_plane = plane_matrices(kernels[:, :, 0], kernels[:, :, 1], cz_here, cx_here)
    adj_plane = plane_matrices(kernels[:, :, 0, ::-1], kernels[:, :, 1, ::-1], cz_here, cx_here)
    lines = lax.optimization_barrier(line_matrices(kernels[:, :, 2], view_shift, cells_y))
    planes = jnp.einsum("vrqp,pj->vrqj", fwd_plane, sent_flat, precision=HIGH)
    images = jnp.einsum("vrqi,vrij->vqj", planes, lines, precision=HIGH) / RANK
    images = images.reshape(VIEWS, cz_here, cx_here, cells_y)
    flags = intersection[:, brick_z, brick_x]
    ratios = jnp.where(
        flags[:, None, None, None] > 0,
        observed.astype(jnp.float32) / (images + BACKGROUND),
        1.0,
    ).astype(jnp.bfloat16)
    ratio_pad = extended(ratios, (("bz", 1), ("bxy", 2)), RADIUS)
    ratio_flat = ratio_pad.astype(jnp.float32).reshape(VIEWS, rows_pad, cells_y)
    spread = jnp.einsum("vrqp,vpj->vrqj", adj_plane, ratio_flat, precision=HIGH)
    correction = jnp.einsum("vrqi,vrji->qj", spread, lines, precision=HIGH) / RANK
    correction = correction.reshape(cz_here, cx_here, cells_y)
    return smoothed * correction / VIEWS


def solution(mesh):
    return jax.shard_map(
        local,
        mesh=mesh,
        in_specs=(P("bz", "bxy", None), P(None, "bz", "bxy", None), P(), P(), P()),
        out_specs=P("bz", "bxy", None),
        check_vma=False,
    )
```

```python
import jax
import jax.numpy as jnp
from jax import lax
from jax.sharding import PartitionSpec as P

VIEWS = 3
RANK = 3
RADIUS = 4
PASSES = 8


EPS_TV = 0.25
TAU = 0.08
BACKGROUND = 0.1
HIGHEST = lax.Precision.HIGHEST
HIGH = lax.Precision.HIGH


def extended(cells, sides, width):
    for axis, dim in sides:
        count = lax.axis_size(axis)
        ends = count - 1
        head = lax.slice_in_dim(cells, 0, width, axis=dim)
        tail = lax.slice_in_dim(cells, cells.shape[dim] - width, cells.shape[dim], axis=dim)
        cells = jnp.concatenate(
            [
                lax.ppermute(tail, axis, [(i, (i + 1) % count) for i in range(ends)]),
                cells,
                lax.ppermute(head, axis, [((i + 1) % count, i) for i in range(ends)]),
            ],
            axis=dim,
        )
    return cells


def tv_pass(padded, z_inside, x_inside):
    field = padded[1:-1, 1:-1]
    z_inside = z_inside[:, None, None]
    x_inside = x_inside[None, :, None]
    y_lower = jnp.concatenate([field[:, :, :1], field[:, :, :-1]], axis=2)
    y_upper = jnp.concatenate([field[:, :, 1:], field[:, :, -1:]], axis=2)
    pairs = (
        (padded[:-2, 1:-1], z_inside[:-2]),
        (padded[2:, 1:-1], z_inside[2:]),
        (padded[1:-1, :-2], x_inside[:, :-2]),
        (padded[1:-1, 2:], x_inside[:, 2:]),
        (y_lower, True),
        (y_upper, True),
    )
    total = jnp.zeros_like(field)
    for beside, inside in pairs:
        diff = beside - field
        total = total + jnp.where(inside, diff / jnp.sqrt(diff * diff + EPS_TV), 0.0)
    return field + TAU * total


def band(taps, rows, cols):
    gap = lax.iota(jnp.int32, cols)[None, :] - lax.iota(jnp.int32, rows)[:, None]
    out = jnp.zeros(taps.shape[:-1] + (rows, cols), jnp.float32)
    for tap in range(taps.shape[-1]):
        out = out + jnp.where(gap == tap, taps[..., tap, None, None], 0.0)
    return out


def plane_matrices(kz, kx, cz, cx):
    wz = band(kz, cz, cz + 2 * RADIUS)
    wx = band(kx, cx, cx + 2 * RADIUS)
    wide = cx + 2 * RADIUS
    q = lax.iota(jnp.int32, cz * cx)
    p = lax.iota(jnp.int32, (cz + 2 * RADIUS) * wide)
    pick_qz = (q[:, None] // cx == lax.iota(jnp.int32, cz)[None, :]).astype(jnp.float32)
    pick_qx = (q[:, None] % cx == lax.iota(jnp.int32, cx)[None, :]).astype(jnp.float32)
    pick_pz = (lax.iota(jnp.int32, cz + 2 * RADIUS)[:, None] == p[None, :] // wide).astype(jnp.float32)
    pick_px = (lax.iota(jnp.int32, wide)[:, None] == p[None, :] % wide).astype(jnp.float32)
    full_z = jnp.einsum("qa,...ab,bp->...qp", pick_qz, wz, pick_pz, precision=HIGHEST)
    full_x = jnp.einsum("qa,...ab,bp->...qp", pick_qx, wx, pick_px, precision=HIGHEST)
    return full_z * full_x


def along_y(values, taps, block):
    cells_y = values.shape[-1]
    wide = block + 2 * RADIUS
    padded = jnp.pad(values, [(0, 0)] * (values.ndim - 1) + [(RADIUS, RADIUS)])
    windows = jnp.stack(
        [padded[..., start:start + wide] for start in range(0, cells_y, block)], axis=-3
    )
    matrix = band(taps, block, wide)
    out = jnp.einsum("vrcqa,vrba->vqcb", windows, matrix, precision=HIGH)
    return out.reshape(out.shape[:2] + (cells_y,))


def local(estimate, observed, psf_taps, view_shift, intersection):
    cz_here, cx_here, cells_y = estimate.shape
    bricks_z = lax.axis_size("bz")
    bricks_x = lax.axis_size("bxy")
    cells_z = cz_here * bricks_z
    cells_x = cx_here * bricks_x
    brick_z = lax.axis_index("bz")
    brick_x = lax.axis_index("bxy")
    z_base = brick_z * cz_here
    x_base = brick_x * cx_here
    smoothed = extended(estimate, (("bz", 0), ("bxy", 1)), PASSES)
    zcoords = z_base - PASSES + lax.iota(jnp.int32, smoothed.shape[0])
    xcoords = x_base - PASSES + lax.iota(jnp.int32, smoothed.shape[1])
    z_mask = (zcoords >= 0) & (zcoords < cells_z)
    x_mask = (xcoords >= 0) & (xcoords < cells_x)
    for pass_index in range(PASSES):
        size_z = smoothed.shape[0]
        size_x = smoothed.shape[1]
        smoothed = tv_pass(
            smoothed,
            z_mask[pass_index:pass_index + size_z],
            x_mask[pass_index:pass_index + size_x],
        )
    sent = smoothed.astype(jnp.bfloat16)
    sent_pad = extended(sent, (("bz", 0), ("bxy", 1)), RADIUS)
    rows_pad = (cz_here + 2 * RADIUS) * (cx_here + 2 * RADIUS)
    rows = cz_here * cx_here
    sent_flat = sent_pad.astype(jnp.float32).reshape(rows_pad, cells_y)
    kernels = psf_taps / jnp.sum(psf_taps, axis=-1, keepdims=True)
    fwd_plane = plane_matrices(kernels[:, :, 0], kernels[:, :, 1], cz_here, cx_here)
    adj_plane = plane_matrices(kernels[:, :, 0, ::-1], kernels[:, :, 1, ::-1], cz_here, cx_here)
    planes = jnp.einsum("vrqp,pj->vrqj", fwd_plane, sent_flat, precision=HIGH)
    planes = jnp.stack([jnp.roll(planes[view], view_shift[view], axis=-1) for view in range(VIEWS)])
    images = along_y(planes, kernels[:, :, 2], 128) / RANK
    images = images.reshape(VIEWS, cz_here, cx_here, cells_y)
    flags = intersection[:, brick_z, brick_x]
    ratios = jnp.where(
        flags[:, None, None, None] > 0,
        observed.astype(jnp.float32) / (images + BACKGROUND),
        1.0,
    ).astype(jnp.bfloat16)
    ratio_pad = extended(ratios, (("bz", 1), ("bxy", 2)), RADIUS)
    ratio_flat = ratio_pad.astype(jnp.float32).reshape(VIEWS, rows_pad, cells_y)
    spread = jnp.einsum("vrqp,vpj->vrqj", adj_plane, ratio_flat, precision=HIGH)
    backs = along_y(spread, kernels[:, :, 2, ::-1], 128)
    correction = sum(jnp.roll(backs[view], -view_shift[view], axis=-1) for view in range(VIEWS)) / RANK
    correction = correction.reshape(cz_here, cx_here, cells_y)
    return smoothed * correction / VIEWS


def solution(mesh):
    return jax.shard_map(
        local,
        mesh=mesh,
        in_specs=(P("bz", "bxy", None), P(None, "bz", "bxy", None), P(), P(), P()),
        out_specs=P("bz", "bxy", None),
        check_vma=False,
    )
```

```python
import jax
import jax.numpy as jnp
from jax import lax
from jax.sharding import PartitionSpec as P

VIEWS = 3
RANK = 3
RADIUS = 4
PASSES = 8


EPS_TV = 0.25
TAU = 0.08
BACKGROUND = 0.1
HIGHEST = lax.Precision.HIGHEST
HIGH = lax.Precision.HIGH


def extended(cells, sides, width):
    for axis, dim in sides:
        count = lax.axis_size(axis)
        ends = count - 1
        head = lax.slice_in_dim(cells, 0, width, axis=dim)
        tail = lax.slice_in_dim(cells, cells.shape[dim] - width, cells.shape[dim], axis=dim)
        cells = jnp.concatenate(
            [
                lax.ppermute(tail, axis, [(i, (i + 1) % count) for i in range(ends)]),
                cells,
                lax.ppermute(head, axis, [((i + 1) % count, i) for i in range(ends)]),
            ],
            axis=dim,
        )
    return cells


def tv_pass(padded, z_first, x_first, cells_z, cells_x):
    field = padded[1:-1, 1:-1]
    below_z = lax.broadcasted_iota(jnp.int32, field.shape, 0) + z_first
    below_x = lax.broadcasted_iota(jnp.int32, field.shape, 1) + x_first
    y_lower = jnp.concatenate([field[:, :, :1], field[:, :, :-1]], axis=2)
    y_upper = jnp.concatenate([field[:, :, 1:], field[:, :, -1:]], axis=2)
    pairs = (
        (padded[:-2, 1:-1], below_z >= 0),
        (padded[2:, 1:-1], below_z + 2 < cells_z),
        (padded[1:-1, :-2], below_x >= 0),
        (padded[1:-1, 2:], below_x + 2 < cells_x),
        (y_lower, True),
        (y_upper, True),
    )
    total = jnp.zeros_like(field)
    for beside, inside in pairs:
        diff = beside - field
        total = total + jnp.where(inside, diff / jnp.sqrt(diff * diff + EPS_TV), 0.0)
    return field + TAU * total


def band(taps, rows, cols):
    gap = lax.iota(jnp.int32, cols)[None, :] - lax.iota(jnp.int32, rows)[:, None]
    out = jnp.zeros(taps.shape[:-1] + (rows, cols), jnp.float32)
    for tap in range(taps.shape[-1]):
        out = out + jnp.where(gap == tap, taps[..., tap, None, None], 0.0)
    return out


def plane_matrices(kz, kx, cz, cx):
    wz = band(kz, cz, cz + 2 * RADIUS)
    wx = band(kx, cx, cx + 2 * RADIUS)
    wide = cx + 2 * RADIUS
    q = lax.iota(jnp.int32, cz * cx)
    p = lax.iota(jnp.int32, (cz + 2 * RADIUS) * wide)
    pick_qz = (q[:, None] // cx == lax.iota(jnp.int32, cz)[None, :]).astype(jnp.float32)
    pick_qx = (q[:, None] % cx == lax.iota(jnp.int32, cx)[None, :]).astype(jnp.float32)
    pick_pz = (lax.iota(jnp.int32, cz + 2 * RADIUS)[:, None] == p[None, :] // wide).astype(jnp.float32)
    pick_px = (lax.iota(jnp.int32, wide)[:, None] == p[None, :] % wide).astype(jnp.float32)
    full_z = jnp.einsum("qa,...ab,bp->...qp", pick_qz, wz, pick_pz, precision=HIGHEST)
    full_x = jnp.einsum("qa,...ab,bp->...qp", pick_qx, wx, pick_px, precision=HIGHEST)
    return full_z * full_x


def line_matrices(ky, shift, ny):
    rows = lax.iota(jnp.int32, ny)[None, :, None] + shift[:, None, None]
    rows = jnp.where(rows >= ny, rows - ny, rows)
    gap = rows - lax.iota(jnp.int32, ny)[None, None, :] + RADIUS
    gap = gap[:, None]
    out = jnp.zeros(ky.shape[:-1] + (ny, ny), jnp.float32)
    for tap in range(ky.shape[-1]):
        out = out + jnp.where(gap == tap, ky[..., tap, None, None], 0.0)
    return out


def local(estimate, observed, psf_taps, view_shift, intersection):
    cz_here, cx_here, cells_y = estimate.shape
    bricks_z = lax.axis_size("bz")
    bricks_x = lax.axis_size("bxy")
    cells_z = cz_here * bricks_z
    cells_x = cx_here * bricks_x
    brick_z = lax.axis_index("bz")
    brick_x = lax.axis_index("bxy")
    z_base = brick_z * cz_here
    x_base = brick_x * cx_here
    smoothed = extended(estimate, (("bz", 0),), PASSES)
    smoothed, view_shift = lax.optimization_barrier((smoothed, view_shift))
    smoothed = extended(smoothed, (("bxy", 1),), PASSES)
    for pass_index in range(PASSES):
        reach = PASSES - pass_index
        smoothed = tv_pass(smoothed, z_base - reach, x_base - reach, cells_z, cells_x)
    sent = smoothed.astype(jnp.bfloat16)
    sent_pad = extended(sent, (("bz", 0), ("bxy", 1)), RADIUS)
    rows_pad = (cz_here + 2 * RADIUS) * (cx_here + 2 * RADIUS)
    rows = cz_here * cx_here
    sent_flat = sent_pad.astype(jnp.float32).reshape(rows_pad, cells_y)
    kernels = psf_taps / jnp.sum(psf_taps, axis=-1, keepdims=True)
    fwd_plane = plane_matrices(kernels[:, :, 0], kernels[:, :, 1], cz_here, cx_here)
    adj_plane = plane_matrices(kernels[:, :, 0, ::-1], kernels[:, :, 1, ::-1], cz_here, cx_here)
    lines = lax.optimization_barrier(line_matrices(kernels[:, :, 2], view_shift, cells_y))
    planes = jnp.einsum("vrqp,pj->vrqj", fwd_plane, sent_flat, precision=HIGH)
    images = jnp.einsum("vrqi,vrij->vqj", planes, lines, precision=HIGH) / RANK
    images = images.reshape(VIEWS, cz_here, cx_here, cells_y)
    flags = intersection[:, brick_z, brick_x]
    ratios = jnp.where(
        flags[:, None, None, None] > 0,
        observed.astype(jnp.float32) / (images + BACKGROUND),
        1.0,
    ).astype(jnp.bfloat16)
    ratio_pad = extended(ratios, (("bz", 1), ("bxy", 2)), RADIUS)
    ratio_flat = ratio_pad.astype(jnp.float32).reshape(VIEWS, rows_pad, cells_y)
    spread = jnp.einsum("vrqp,vpj->vrqj", adj_plane, ratio_flat, precision=HIGH)
    correction = jnp.einsum("vrqi,vrji->qj", spread, lines, precision=HIGH) / RANK
    correction = correction.reshape(cz_here, cx_here, cells_y)
    return smoothed * correction / VIEWS


def solution(mesh):
    return jax.shard_map(
        local,
        mesh=mesh,
        in_specs=(P("bz", "bxy", None), P(None, "bz", "bxy", None), P(), P(), P()),
        out_specs=P("bz", "bxy", None),
        check_vma=False,
    )
```

```python
import jax
import jax.numpy as jnp
from jax import lax
from jax.sharding import PartitionSpec as P

VIEWS = 3
RANK = 3
RADIUS = 4
PASSES = 8


EPS_TV = 0.25
TAU = 0.08
BACKGROUND = 0.1
HIGHEST = lax.Precision.HIGHEST
HIGH = lax.Precision.HIGH


def extended(cells, sides, width):
    for axis, dim in sides:
        count = lax.axis_size(axis)
        ends = count - 1
        head = lax.slice_in_dim(cells, 0, width, axis=dim)
        tail = lax.slice_in_dim(cells, cells.shape[dim] - width, cells.shape[dim], axis=dim)
        cells = jnp.concatenate(
            [
                lax.ppermute(tail, axis, [(i, (i + 1) % count) for i in range(ends)]),
                cells,
                lax.ppermute(head, axis, [((i + 1) % count, i) for i in range(ends)]),
            ],
            axis=dim,
        )
    return cells


def flux(diff):
    return diff / jnp.sqrt(diff * diff + EPS_TV)


def tv_pass(padded, z_first, x_first, cells_z, cells_x):
    field = padded[1:-1, 1:-1]
    below_z = lax.broadcasted_iota(jnp.int32, field.shape, 0) + z_first
    below_x = lax.broadcasted_iota(jnp.int32, field.shape, 1) + x_first
    along_j = lax.broadcasted_iota(jnp.int32, field.shape, 2)
    step_z = flux(padded[1:, 1:-1] - padded[:-1, 1:-1])
    step_x = flux(padded[1:-1, 1:] - padded[1:-1, :-1])
    step_y = flux(field[:, :, 1:] - field[:, :, :-1])
    cells_y = field.shape[2]
    pad_y = jnp.zeros(field.shape[:2] + (1,), field.dtype)
    up_y = jnp.concatenate([step_y, pad_y], axis=2)
    down_y = jnp.concatenate([pad_y, step_y], axis=2)
    terms = (
        (-step_z[:-1], below_z >= 0),
        (step_z[1:], below_z + 2 < cells_z),
        (-step_x[:, :-1], below_x >= 0),
        (step_x[:, 1:], below_x + 2 < cells_x),
        (-down_y, along_j >= 1),
        (up_y, along_j < cells_y - 1),
    )
    total = jnp.zeros_like(field)
    for term, inside in terms:
        total = total + jnp.where(inside, term, 0.0)
    return field + TAU * total


def band(taps, rows, cols):
    gap = lax.iota(jnp.int32, cols)[None, :] - lax.iota(jnp.int32, rows)[:, None]
    out = jnp.zeros(taps.shape[:-1] + (rows, cols), jnp.float32)
    for tap in range(taps.shape[-1]):
        out = out + jnp.where(gap == tap, taps[..., tap, None, None], 0.0)
    return out


def plane_matrices(kz, kx, cz, cx):
    wz = band(kz, cz, cz + 2 * RADIUS)
    wx = band(kx, cx, cx + 2 * RADIUS)
    wide = cx + 2 * RADIUS
    q = lax.iota(jnp.int32, cz * cx)
    p = lax.iota(jnp.int32, (cz + 2 * RADIUS) * wide)
    pick_qz = (q[:, None] // cx == lax.iota(jnp.int32, cz)[None, :]).astype(jnp.float32)
    pick_qx = (q[:, None] % cx == lax.iota(jnp.int32, cx)[None, :]).astype(jnp.float32)
    pick_pz = (lax.iota(jnp.int32, cz + 2 * RADIUS)[:, None] == p[None, :] // wide).astype(jnp.float32)
    pick_px = (lax.iota(jnp.int32, wide)[:, None] == p[None, :] % wide).astype(jnp.float32)
    full_z = jnp.einsum("qa,...ab,bp->...qp", pick_qz, wz, pick_pz, precision=HIGHEST)
    full_x = jnp.einsum("qa,...ab,bp->...qp", pick_qx, wx, pick_px, precision=HIGHEST)
    return full_z * full_x


def line_matrices(ky, shift, ny):
    rows = lax.iota(jnp.int32, ny)[None, :, None] + shift[:, None, None]
    rows = jnp.where(rows >= ny, rows - ny, rows)
    gap = rows - lax.iota(jnp.int32, ny)[None, None, :] + RADIUS
    gap = gap[:, None]
    out = jnp.zeros(ky.shape[:-1] + (ny, ny), jnp.float32)
    for tap in range(ky.shape[-1]):
        out = out + jnp.where(gap == tap, ky[..., tap, None, None], 0.0)
    return out


def local(estimate, observed, psf_taps, view_shift, intersection):
    cz_here, cx_here, cells_y = estimate.shape
    bricks_z = lax.axis_size("bz")
    bricks_x = lax.axis_size("bxy")
    cells_z = cz_here * bricks_z
    cells_x = cx_here * bricks_x
    brick_z = lax.axis_index("bz")
    brick_x = lax.axis_index("bxy")
    z_base = brick_z * cz_here
    x_base = brick_x * cx_here
    smoothed = extended(estimate, (("bxy", 1),), PASSES)
    smoothed, view_shift = lax.optimization_barrier((smoothed, view_shift))
    smoothed = extended(smoothed, (("bz", 0),), PASSES)
    for pass_index in range(PASSES):
        reach = PASSES - pass_index
        smoothed = tv_pass(smoothed, z_base - reach, x_base - reach, cells_z, cells_x)
    sent = smoothed.astype(jnp.bfloat16)
    sent_pad = extended(sent, (("bz", 0), ("bxy", 1)), RADIUS)
    rows_pad = (cz_here + 2 * RADIUS) * (cx_here + 2 * RADIUS)
    rows = cz_here * cx_here
    sent_flat = sent_pad.astype(jnp.float32).reshape(rows_pad, cells_y)
    kernels = psf_taps / jnp.sum(psf_taps, axis=-1, keepdims=True)
    fwd_plane = plane_matrices(kernels[:, :, 0], kernels[:, :, 1], cz_here, cx_here)
    adj_plane = plane_matrices(kernels[:, :, 0, ::-1], kernels[:, :, 1, ::-1], cz_here, cx_here)
    lines = lax.optimization_barrier(line_matrices(kernels[:, :, 2], view_shift, cells_y))
    planes = jnp.einsum("vrqp,pj->vrqj", fwd_plane, sent_flat, precision=HIGH)
    images = jnp.einsum("vrqi,vrij->vqj", planes, lines, precision=HIGH) / RANK
    images = images.reshape(VIEWS, cz_here, cx_here, cells_y)
    flags = intersection[:, brick_z, brick_x]
    ratios = jnp.where(
        flags[:, None, None, None] > 0,
        observed.astype(jnp.float32) / (images + BACKGROUND),
        1.0,
    ).astype(jnp.bfloat16)
    ratio_pad = extended(ratios, (("bz", 1), ("bxy", 2)), RADIUS)
    ratio_flat = ratio_pad.astype(jnp.float32).reshape(VIEWS, rows_pad, cells_y)
    spread = jnp.einsum("vrqp,vpj->vrqj", adj_plane, ratio_flat, precision=HIGH)
    correction = jnp.einsum("vrqi,vrji->qj", spread, lines, precision=HIGH) / RANK
    correction = correction.reshape(cz_here, cx_here, cells_y)
    return smoothed * correction / VIEWS


def solution(mesh):
    return jax.shard_map(
        local,
        mesh=mesh,
        in_specs=(P("bz", "bxy", None), P(None, "bz", "bxy", None), P(), P(), P()),
        out_specs=P("bz", "bxy", None),
        check_vma=False,
    )
```

```python
import jax
import jax.numpy as jnp
from jax import lax
from jax.sharding import PartitionSpec as P

VIEWS = 3
RANK = 3
RADIUS = 4
PASSES = 8


EPS_TV = 0.25
TAU = 0.08
BACKGROUND = 0.1
HIGHEST = lax.Precision.HIGHEST
HIGH = lax.Precision.HIGH


def extended(cells, sides, width):
    for axis, dim in sides:
        count = lax.axis_size(axis)
        ends = count - 1
        head = lax.slice_in_dim(cells, 0, width, axis=dim)
        tail = lax.slice_in_dim(cells, cells.shape[dim] - width, cells.shape[dim], axis=dim)
        cells = jnp.concatenate(
            [
                lax.ppermute(tail, axis, [(i, (i + 1) % count) for i in range(ends)]),
                cells,
                lax.ppermute(head, axis, [((i + 1) % count, i) for i in range(ends)]),
            ],
            axis=dim,
        )
    return cells


def flux(diff):
    return diff / jnp.sqrt(diff * diff + EPS_TV)


def tv_pass(padded, z_first, x_first, cells_z, cells_x):
    field = padded[1:-1, 1:-1]
    below_z = lax.broadcasted_iota(jnp.int32, field.shape, 0) + z_first
    below_x = lax.broadcasted_iota(jnp.int32, field.shape, 1) + x_first
    along_j = lax.broadcasted_iota(jnp.int32, field.shape, 2)
    step_z = flux(padded[1:, 1:-1] - padded[:-1, 1:-1])
    step_x = flux(padded[1:-1, 1:] - padded[1:-1, :-1])
    step_y = flux(field[:, :, 1:] - field[:, :, :-1])
    cells_y = field.shape[2]
    pad_y = jnp.zeros(field.shape[:2] + (1,), field.dtype)
    up_y = jnp.concatenate([step_y, pad_y], axis=2)
    down_y = jnp.concatenate([pad_y, step_y], axis=2)
    terms = (
        (-step_z[:-1], below_z >= 0),
        (step_z[1:], below_z + 2 < cells_z),
        (-step_x[:, :-1], below_x >= 0),
        (step_x[:, 1:], below_x + 2 < cells_x),
        (-down_y, along_j >= 1),
        (up_y, along_j < cells_y - 1),
    )
    total = jnp.zeros_like(field)
    for term, inside in terms:
        total = total + jnp.where(inside, term, 0.0)
    return field + TAU * total


def band(taps, rows, cols):
    gap = lax.iota(jnp.int32, cols)[None, :] - lax.iota(jnp.int32, rows)[:, None]
    out = jnp.zeros(taps.shape[:-1] + (rows, cols), jnp.float32)
    for tap in range(taps.shape[-1]):
        out = out + jnp.where(gap == tap, taps[..., tap, None, None], 0.0)
    return out


def plane_matrices(kz, kx, cz, cx):
    wz = band(kz, cz, cz + 2 * RADIUS)
    wx = band(kx, cx, cx + 2 * RADIUS)
    wide = cx + 2 * RADIUS
    q = lax.iota(jnp.int32, cz * cx)
    p = lax.iota(jnp.int32, (cz + 2 * RADIUS) * wide)
    pick_qz = (q[:, None] // cx == lax.iota(jnp.int32, cz)[None, :]).astype(jnp.float32)
    pick_qx = (q[:, None] % cx == lax.iota(jnp.int32, cx)[None, :]).astype(jnp.float32)
    pick_pz = (lax.iota(jnp.int32, cz + 2 * RADIUS)[:, None] == p[None, :] // wide).astype(jnp.float32)
    pick_px = (lax.iota(jnp.int32, wide)[:, None] == p[None, :] % wide).astype(jnp.float32)
    full_z = jnp.einsum("qa,...ab,bp->...qp", pick_qz, wz, pick_pz, precision=HIGHEST)
    full_x = jnp.einsum("qa,...ab,bp->...qp", pick_qx, wx, pick_px, precision=HIGHEST)
    return full_z * full_x


def line_matrices(ky, shift, ny):
    rows = lax.iota(jnp.int32, ny)[None, :, None] + shift[:, None, None]
    rows = jnp.where(rows >= ny, rows - ny, rows)
    gap = rows - lax.iota(jnp.int32, ny)[None, None, :] + RADIUS
    gap = gap[:, None]
    out = jnp.zeros(ky.shape[:-1] + (ny, ny), jnp.float32)
    for tap in range(ky.shape[-1]):
        out = out + jnp.where(gap == tap, ky[..., tap, None, None], 0.0)
    return out


def local(estimate, observed, psf_taps, view_shift, intersection):
    cz_here, cx_here, cells_y = estimate.shape
    bricks_z = lax.axis_size("bz")
    bricks_x = lax.axis_size("bxy")
    cells_z = cz_here * bricks_z
    cells_x = cx_here * bricks_x
    brick_z = lax.axis_index("bz")
    brick_x = lax.axis_index("bxy")
    z_base = brick_z * cz_here
    x_base = brick_x * cx_here
    smoothed = extended(estimate, (("bz", 0),), PASSES)
    smoothed, view_shift, psf_taps = lax.optimization_barrier((smoothed, view_shift, psf_taps))
    kernels = psf_taps / jnp.sum(psf_taps, axis=-1, keepdims=True)
    lines = line_matrices(kernels[:, :, 2], view_shift, cells_y)
    smoothed = extended(smoothed, (("bxy", 1),), PASSES)
    smoothed, lines = lax.optimization_barrier((smoothed, lines))
    for pass_index in range(PASSES):
        reach = PASSES - pass_index
        smoothed = tv_pass(smoothed, z_base - reach, x_base - reach, cells_z, cells_x)
    sent = smoothed.astype(jnp.bfloat16)
    sent_pad = extended(sent, (("bz", 0), ("bxy", 1)), RADIUS)
    rows_pad = (cz_here + 2 * RADIUS) * (cx_here + 2 * RADIUS)
    rows = cz_here * cx_here
    sent_flat = sent_pad.astype(jnp.float32).reshape(rows_pad, cells_y)
    fwd_plane = plane_matrices(kernels[:, :, 0], kernels[:, :, 1], cz_here, cx_here)
    adj_plane = plane_matrices(kernels[:, :, 0, ::-1], kernels[:, :, 1, ::-1], cz_here, cx_here)
    planes = jnp.einsum("vrqp,pj->vrqj", fwd_plane, sent_flat, precision=HIGH)
    images = jnp.einsum("vrqi,vrij->vqj", planes, lines, precision=HIGH) / RANK
    images = images.reshape(VIEWS, cz_here, cx_here, cells_y)
    flags = intersection[:, brick_z, brick_x]
    ratios = jnp.where(
        flags[:, None, None, None] > 0,
        observed.astype(jnp.float32) / (images + BACKGROUND),
        1.0,
    ).astype(jnp.bfloat16)
    ratio_pad = extended(ratios, (("bz", 1), ("bxy", 2)), RADIUS)
    ratio_flat = ratio_pad.astype(jnp.float32).reshape(VIEWS, rows_pad, cells_y)
    spread = jnp.einsum("vrqp,vpj->vrqj", adj_plane, ratio_flat, precision=HIGH)
    correction = jnp.einsum("vrqi,vrji->qj", spread, lines, precision=HIGH) / RANK
    correction = correction.reshape(cz_here, cx_here, cells_y)
    return smoothed * correction / VIEWS


def solution(mesh):
    return jax.shard_map(
        local,
        mesh=mesh,
        in_specs=(P("bz", "bxy", None), P(None, "bz", "bxy", None), P(), P(), P()),
        out_specs=P("bz", "bxy", None),
        check_vma=False,
    )
```

```python
import jax
import jax.numpy as jnp
from jax import lax
from jax.sharding import PartitionSpec as P

VIEWS = 3
RANK = 3
RADIUS = 4
PASSES = 8


EPS_TV = 0.25
TAU = 0.08
BACKGROUND = 0.1
HIGHEST = lax.Precision.HIGHEST
HIGH = lax.Precision.HIGH


def extended(cells, sides, width):
    for axis, dim in sides:
        count = lax.axis_size(axis)
        ends = count - 1
        head = lax.slice_in_dim(cells, 0, width, axis=dim)
        tail = lax.slice_in_dim(cells, cells.shape[dim] - width, cells.shape[dim], axis=dim)
        cells = jnp.concatenate(
            [
                lax.ppermute(tail, axis, [(i, (i + 1) % count) for i in range(ends)]),
                cells,
                lax.ppermute(head, axis, [((i + 1) % count, i) for i in range(ends)]),
            ],
            axis=dim,
        )
    return cells


def flux(diff):
    return diff / jnp.sqrt(diff * diff + EPS_TV)


def tv_pass(padded, z_lower, z_upper, x_lower, x_upper):
    field = padded[1:-1, 1:-1]
    cells_y = field.shape[2]
    along_j = lax.broadcasted_iota(jnp.int32, field.shape, 2)
    step_z = flux(padded[1:, 1:-1] - padded[:-1, 1:-1])
    step_x = flux(padded[1:-1, 1:] - padded[1:-1, :-1])
    step_y = flux(field[:, :, 1:] - field[:, :, :-1])
    pad_y = jnp.zeros(field.shape[:2] + (1,), field.dtype)
    up_y = jnp.concatenate([step_y, pad_y], axis=2)
    down_y = jnp.concatenate([pad_y, step_y], axis=2)
    total = jnp.zeros_like(field)
    total = total + -step_z[:-1] * z_lower[:, None, None]
    total = total + step_z[1:] * z_upper[:, None, None]
    total = total + -step_x[:, :-1] * x_lower[None, :, None]
    total = total + step_x[:, 1:] * x_upper[None, :, None]
    total = total + jnp.where(along_j >= 1, -down_y, 0.0)
    total = total + jnp.where(along_j < cells_y - 1, up_y, 0.0)
    return field + TAU * total


def band(taps, rows, cols):
    gap = lax.iota(jnp.int32, cols)[None, :] - lax.iota(jnp.int32, rows)[:, None]
    out = jnp.zeros(taps.shape[:-1] + (rows, cols), jnp.float32)
    for tap in range(taps.shape[-1]):
        out = out + jnp.where(gap == tap, taps[..., tap, None, None], 0.0)
    return out


def plane_matrices(kz, kx, cz, cx):
    wz = band(kz, cz, cz + 2 * RADIUS)
    wx = band(kx, cx, cx + 2 * RADIUS)
    wide = cx + 2 * RADIUS
    q = lax.iota(jnp.int32, cz * cx)
    p = lax.iota(jnp.int32, (cz + 2 * RADIUS) * wide)
    pick_qz = (q[:, None] // cx == lax.iota(jnp.int32, cz)[None, :]).astype(jnp.float32)
    pick_qx = (q[:, None] % cx == lax.iota(jnp.int32, cx)[None, :]).astype(jnp.float32)
    pick_pz = (lax.iota(jnp.int32, cz + 2 * RADIUS)[:, None] == p[None, :] // wide).astype(jnp.float32)
    pick_px = (lax.iota(jnp.int32, wide)[:, None] == p[None, :] % wide).astype(jnp.float32)
    full_z = jnp.einsum("qa,...ab,bp->...qp", pick_qz, wz, pick_pz, precision=HIGHEST)
    full_x = jnp.einsum("qa,...ab,bp->...qp", pick_qx, wx, pick_px, precision=HIGHEST)
    return full_z * full_x


def line_matrices(ky, shift, ny):
    rows = lax.iota(jnp.int32, ny)[None, :, None] + shift[:, None, None]
    rows = jnp.where(rows >= ny, rows - ny, rows)
    gap = rows - lax.iota(jnp.int32, ny)[None, None, :] + RADIUS
    gap = gap[:, None]
    out = jnp.zeros(ky.shape[:-1] + (ny, ny), jnp.float32)
    for tap in range(ky.shape[-1]):
        out = out + jnp.where(gap == tap, ky[..., tap, None, None], 0.0)
    return out


def local(estimate, observed, psf_taps, view_shift, intersection):
    cz_here, cx_here, cells_y = estimate.shape
    bricks_z = lax.axis_size("bz")
    bricks_x = lax.axis_size("bxy")
    cells_z = cz_here * bricks_z
    cells_x = cx_here * bricks_x
    brick_z = lax.axis_index("bz")
    brick_x = lax.axis_index("bxy")
    z_base = brick_z * cz_here
    x_base = brick_x * cx_here
    smoothed = extended(estimate, (("bz", 0),), PASSES)
    smoothed, view_shift = lax.optimization_barrier((smoothed, view_shift))
    smoothed = extended(smoothed, (("bxy", 1),), PASSES)
    zc = z_base - PASSES + lax.iota(jnp.int32, smoothed.shape[0])
    xc = x_base - PASSES + lax.iota(jnp.int32, smoothed.shape[1])
    masks = lax.optimization_barrier((
        ((zc >= 0) & (zc < cells_z)).astype(jnp.float32),
        ((xc >= 0) & (xc < cells_x)).astype(jnp.float32),
    ))
    z_in, x_in = masks
    for pass_index in range(PASSES):
        size_z = smoothed.shape[0] - 2
        size_x = smoothed.shape[1] - 2
        z0 = pass_index
        x0 = pass_index
        smoothed = tv_pass(
            smoothed,
            z_in[z0:z0 + size_z],
            z_in[z0 + 2:z0 + 2 + size_z],
            x_in[x0:x0 + size_x],
            x_in[x0 + 2:x0 + 2 + size_x],
        )
    sent = smoothed.astype(jnp.bfloat16)
    sent_pad = extended(sent, (("bz", 0), ("bxy", 1)), RADIUS)
    rows_pad = (cz_here + 2 * RADIUS) * (cx_here + 2 * RADIUS)
    rows = cz_here * cx_here
    sent_flat = sent_pad.astype(jnp.float32).reshape(rows_pad, cells_y)
    kernels = psf_taps / jnp.sum(psf_taps, axis=-1, keepdims=True)
    fwd_plane = plane_matrices(kernels[:, :, 0], kernels[:, :, 1], cz_here, cx_here)
    adj_plane = plane_matrices(kernels[:, :, 0, ::-1], kernels[:, :, 1, ::-1], cz_here, cx_here)
    lines = lax.optimization_barrier(line_matrices(kernels[:, :, 2], view_shift, cells_y))
    planes = jnp.einsum("vrqp,pj->vrqj", fwd_plane, sent_flat, precision=HIGH)
    images = jnp.einsum("vrqi,vrij->vqj", planes, lines, precision=HIGH) / RANK
    images = images.reshape(VIEWS, cz_here, cx_here, cells_y)
    flags = intersection[:, brick_z, brick_x]
    ratios = jnp.where(
        flags[:, None, None, None] > 0,
        observed.astype(jnp.float32) / (images + BACKGROUND),
        1.0,
    ).astype(jnp.bfloat16)
    ratio_pad = extended(ratios, (("bz", 1), ("bxy", 2)), RADIUS)
    ratio_flat = ratio_pad.astype(jnp.float32).reshape(VIEWS, rows_pad, cells_y)
    spread = jnp.einsum("vrqp,vpj->vrqj", adj_plane, ratio_flat, precision=HIGH)
    correction = jnp.einsum("vrqi,vrji->qj", spread, lines, precision=HIGH) / RANK
    correction = correction.reshape(cz_here, cx_here, cells_y)
    return smoothed * correction / VIEWS


def solution(mesh):
    return jax.shard_map(
        local,
        mesh=mesh,
        in_specs=(P("bz", "bxy", None), P(None, "bz", "bxy", None), P(), P(), P()),
        out_specs=P("bz", "bxy", None),
        check_vma=False,
    )
```

```python
import jax
import jax.numpy as jnp
from jax import lax
from jax.sharding import PartitionSpec as P

VIEWS = 3
RANK = 3
RADIUS = 4
PASSES = 8


EPS_TV = 0.25
TAU = 0.08
BACKGROUND = 0.1
HIGHEST = lax.Precision.HIGHEST
HIGH = lax.Precision.HIGH


def extended(cells, sides, width):
    for axis, dim in sides:
        count = lax.axis_size(axis)
        ends = count - 1
        head = lax.slice_in_dim(cells, 0, width, axis=dim)
        tail = lax.slice_in_dim(cells, cells.shape[dim] - width, cells.shape[dim], axis=dim)
        cells = jnp.concatenate(
            [
                lax.ppermute(tail, axis, [(i, (i + 1) % count) for i in range(ends)]),
                cells,
                lax.ppermute(head, axis, [((i + 1) % count, i) for i in range(ends)]),
            ],
            axis=dim,
        )
    return cells


def flux(diff):
    return diff / jnp.sqrt(diff * diff + EPS_TV)


def tv_pass(padded, z_lower, z_upper, x_lower, x_upper):
    field = padded[1:-1, 1:-1]
    cells_y = field.shape[2]
    along_j = lax.broadcasted_iota(jnp.int32, field.shape, 2)
    step_z = flux(padded[1:, 1:-1] - padded[:-1, 1:-1])
    step_x = flux(padded[1:-1, 1:] - padded[1:-1, :-1])
    step_y = flux(field[:, :, 1:] - field[:, :, :-1])
    pad_y = jnp.zeros(field.shape[:2] + (1,), field.dtype)
    up_y = jnp.concatenate([step_y, pad_y], axis=2)
    down_y = jnp.concatenate([pad_y, step_y], axis=2)
    total = jnp.zeros_like(field)
    total = total + -step_z[:-1] * z_lower[:, None, None]
    total = total + step_z[1:] * z_upper[:, None, None]
    total = total + -step_x[:, :-1] * x_lower[None, :, None]
    total = total + step_x[:, 1:] * x_upper[None, :, None]
    total = total + jnp.where(along_j >= 1, -down_y, 0.0)
    total = total + jnp.where(along_j < cells_y - 1, up_y, 0.0)
    return field + TAU * total


def band(taps, rows, cols):
    gap = lax.iota(jnp.int32, cols)[None, :] - lax.iota(jnp.int32, rows)[:, None]
    out = jnp.zeros(taps.shape[:-1] + (rows, cols), jnp.float32)
    for tap in range(taps.shape[-1]):
        out = out + jnp.where(gap == tap, taps[..., tap, None, None], 0.0)
    return out


def plane_matrices(kz, kx, cz, cx):
    wz = band(kz, cz, cz + 2 * RADIUS)
    wx = band(kx, cx, cx + 2 * RADIUS)
    wide = cx + 2 * RADIUS
    q = lax.iota(jnp.int32, cz * cx)
    p = lax.iota(jnp.int32, (cz + 2 * RADIUS) * wide)
    pick_qz = (q[:, None] // cx == lax.iota(jnp.int32, cz)[None, :]).astype(jnp.float32)
    pick_qx = (q[:, None] % cx == lax.iota(jnp.int32, cx)[None, :]).astype(jnp.float32)
    pick_pz = (lax.iota(jnp.int32, cz + 2 * RADIUS)[:, None] == p[None, :] // wide).astype(jnp.float32)
    pick_px = (lax.iota(jnp.int32, wide)[:, None] == p[None, :] % wide).astype(jnp.float32)
    full_z = jnp.einsum("qa,...ab,bp->...qp", pick_qz, wz, pick_pz, precision=HIGHEST)
    full_x = jnp.einsum("qa,...ab,bp->...qp", pick_qx, wx, pick_px, precision=HIGHEST)
    return full_z * full_x


def line_matrices(ky, shift, ny):
    rows = lax.iota(jnp.int32, ny)[None, :, None] + shift[:, None, None]
    rows = jnp.where(rows >= ny, rows - ny, rows)
    gap = rows - lax.iota(jnp.int32, ny)[None, None, :] + RADIUS
    gap = gap[:, None]
    out = jnp.zeros(ky.shape[:-1] + (ny, ny), jnp.float32)
    for tap in range(ky.shape[-1]):
        out = out + jnp.where(gap == tap, ky[..., tap, None, None], 0.0)
    return out


def local(estimate, observed, psf_taps, view_shift, intersection):
    cz_here, cx_here, cells_y = estimate.shape
    bricks_z = lax.axis_size("bz")
    bricks_x = lax.axis_size("bxy")
    cells_z = cz_here * bricks_z
    cells_x = cx_here * bricks_x
    brick_z = lax.axis_index("bz")
    brick_x = lax.axis_index("bxy")
    z_base = brick_z * cz_here
    x_base = brick_x * cx_here
    smoothed = extended(estimate, (("bz", 0),), PASSES)
    smoothed, taps_zx = lax.optimization_barrier((smoothed, psf_taps[:, :, :2]))
    smoothed = extended(smoothed, (("bxy", 1),), PASSES)
    zc = z_base - PASSES + lax.iota(jnp.int32, smoothed.shape[0])
    xc = x_base - PASSES + lax.iota(jnp.int32, smoothed.shape[1])
    masks = lax.optimization_barrier((
        ((zc >= 0) & (zc < cells_z)).astype(jnp.float32),
        ((xc >= 0) & (xc < cells_x)).astype(jnp.float32),
    ))
    z_in, x_in = masks
    for pass_index in range(PASSES):
        size_z = smoothed.shape[0] - 2
        size_x = smoothed.shape[1] - 2
        z0 = pass_index
        x0 = pass_index
        smoothed = tv_pass(
            smoothed,
            z_in[z0:z0 + size_z],
            z_in[z0 + 2:z0 + 2 + size_z],
            x_in[x0:x0 + size_x],
            x_in[x0 + 2:x0 + 2 + size_x],
        )
    smoothed, view_shift = lax.optimization_barrier((smoothed, view_shift))
    sent = smoothed.astype(jnp.bfloat16)
    sent_pad = extended(sent, (("bz", 0), ("bxy", 1)), RADIUS)
    rows_pad = (cz_here + 2 * RADIUS) * (cx_here + 2 * RADIUS)
    rows = cz_here * cx_here
    sent_flat = sent_pad.astype(jnp.float32).reshape(rows_pad, cells_y)
    kernels = psf_taps / jnp.sum(psf_taps, axis=-1, keepdims=True)
    kernels_zx = taps_zx / jnp.sum(taps_zx, axis=-1, keepdims=True)
    fwd_plane = plane_matrices(kernels_zx[:, :, 0], kernels_zx[:, :, 1], cz_here, cx_here)
    adj_plane = plane_matrices(kernels_zx[:, :, 0, ::-1], kernels_zx[:, :, 1, ::-1], cz_here, cx_here)
    lines = lax.optimization_barrier(line_matrices(kernels[:, :, 2], view_shift, cells_y))
    planes = jnp.einsum("vrqp,pj->vrqj", fwd_plane, sent_flat, precision=HIGH)
    images = jnp.einsum("vrqi,vrij->vqj", planes, lines, precision=HIGH) / RANK
    images = images.reshape(VIEWS, cz_here, cx_here, cells_y)
    flags = intersection[:, brick_z, brick_x]
    ratios = jnp.where(
        flags[:, None, None, None] > 0,
        observed.astype(jnp.float32) / (images + BACKGROUND),
        1.0,
    ).astype(jnp.bfloat16)
    ratio_pad = extended(ratios, (("bz", 1), ("bxy", 2)), RADIUS)
    ratio_flat = ratio_pad.astype(jnp.float32).reshape(VIEWS, rows_pad, cells_y)
    spread = jnp.einsum("vrqp,vpj->vrqj", adj_plane, ratio_flat, precision=HIGH)
    correction = jnp.einsum("vrqi,vrji->qj", spread, lines, precision=HIGH) / RANK
    correction = correction.reshape(cz_here, cx_here, cells_y)
    return smoothed * correction / VIEWS


def solution(mesh):
    return jax.shard_map(
        local,
        mesh=mesh,
        in_specs=(P("bz", "bxy", None), P(None, "bz", "bxy", None), P(), P(), P()),
        out_specs=P("bz", "bxy", None),
        check_vma=False,
    )
```

```python
import jax
import jax.numpy as jnp
from jax import lax
from jax.sharding import PartitionSpec as P

VIEWS = 3
RANK = 3
RADIUS = 4
PASSES = 8


EPS_TV = 0.25
TAU = 0.08
BACKGROUND = 0.1
HIGHEST = lax.Precision.HIGHEST
HIGH = lax.Precision.HIGH


def extended(cells, sides, width):
    for axis, dim in sides:
        count = lax.axis_size(axis)
        ends = count - 1
        head = lax.slice_in_dim(cells, 0, width, axis=dim)
        tail = lax.slice_in_dim(cells, cells.shape[dim] - width, cells.shape[dim], axis=dim)
        cells = jnp.concatenate(
            [
                lax.ppermute(tail, axis, [(i, (i + 1) % count) for i in range(ends)]),
                cells,
                lax.ppermute(head, axis, [((i + 1) % count, i) for i in range(ends)]),
            ],
            axis=dim,
        )
    return cells


def flux(diff):
    return diff / jnp.sqrt(diff * diff + EPS_TV)


def tv_pass(padded, z_lower, z_upper, x_lower, x_upper):
    field = padded[1:-1, 1:-1]
    cells_y = field.shape[2]
    along_j = lax.broadcasted_iota(jnp.int32, field.shape, 2)
    step_z = flux(padded[1:, 1:-1] - padded[:-1, 1:-1])
    step_x = flux(padded[1:-1, 1:] - padded[1:-1, :-1])
    step_y = flux(field[:, :, 1:] - field[:, :, :-1])
    pad_y = jnp.zeros(field.shape[:2] + (1,), field.dtype)
    up_y = jnp.concatenate([step_y, pad_y], axis=2)
    down_y = jnp.concatenate([pad_y, step_y], axis=2)
    total = jnp.zeros_like(field)
    total = total + -step_z[:-1] * z_lower[:, None, None]
    total = total + step_z[1:] * z_upper[:, None, None]
    total = total + -step_x[:, :-1] * x_lower[None, :, None]
    total = total + step_x[:, 1:] * x_upper[None, :, None]
    total = total + jnp.where(along_j >= 1, -down_y, 0.0)
    total = total + jnp.where(along_j < cells_y - 1, up_y, 0.0)
    return field + TAU * total


def band(taps, rows, cols):
    gap = lax.iota(jnp.int32, cols)[None, :] - lax.iota(jnp.int32, rows)[:, None]
    out = jnp.zeros(taps.shape[:-1] + (rows, cols), jnp.float32)
    for tap in range(taps.shape[-1]):
        out = out + jnp.where(gap == tap, taps[..., tap, None, None], 0.0)
    return out


def plane_matrices(kz, kx, cz, cx):
    wz = band(kz, cz, cz + 2 * RADIUS)
    wx = band(kx, cx, cx + 2 * RADIUS)
    wide = cx + 2 * RADIUS
    q = lax.iota(jnp.int32, cz * cx)
    p = lax.iota(jnp.int32, (cz + 2 * RADIUS) * wide)
    pick_qz = (q[:, None] // cx == lax.iota(jnp.int32, cz)[None, :]).astype(jnp.float32)
    pick_qx = (q[:, None] % cx == lax.iota(jnp.int32, cx)[None, :]).astype(jnp.float32)
    pick_pz = (lax.iota(jnp.int32, cz + 2 * RADIUS)[:, None] == p[None, :] // wide).astype(jnp.float32)
    pick_px = (lax.iota(jnp.int32, wide)[:, None] == p[None, :] % wide).astype(jnp.float32)
    full_z = jnp.einsum("qa,...ab,bp->...qp", pick_qz, wz, pick_pz, precision=HIGH)
    full_x = jnp.einsum("qa,...ab,bp->...qp", pick_qx, wx, pick_px, precision=HIGH)
    return full_z * full_x


def line_matrices(ky, shift, ny):
    rows = lax.iota(jnp.int32, ny)[None, :, None] + shift[:, None, None]
    rows = jnp.where(rows >= ny, rows - ny, rows)
    gap = rows - lax.iota(jnp.int32, ny)[None, None, :] + RADIUS
    gap = gap[:, None]
    out = jnp.zeros(ky.shape[:-1] + (ny, ny), jnp.float32)
    for tap in range(ky.shape[-1]):
        out = out + jnp.where(gap == tap, ky[..., tap, None, None], 0.0)
    return out


def local(estimate, observed, psf_taps, view_shift, intersection):
    cz_here, cx_here, cells_y = estimate.shape
    bricks_z = lax.axis_size("bz")
    bricks_x = lax.axis_size("bxy")
    cells_z = cz_here * bricks_z
    cells_x = cx_here * bricks_x
    brick_z = lax.axis_index("bz")
    brick_x = lax.axis_index("bxy")
    z_base = brick_z * cz_here
    x_base = brick_x * cx_here
    smoothed = extended(estimate, (("bz", 0),), PASSES)
    smoothed, view_shift = lax.optimization_barrier((smoothed, view_shift))
    smoothed = extended(smoothed, (("bxy", 1),), PASSES)
    zc = z_base - PASSES + lax.iota(jnp.int32, smoothed.shape[0])
    xc = x_base - PASSES + lax.iota(jnp.int32, smoothed.shape[1])
    masks = lax.optimization_barrier((
        ((zc >= 0) & (zc < cells_z)).astype(jnp.float32),
        ((xc >= 0) & (xc < cells_x)).astype(jnp.float32),
    ))
    z_in, x_in = masks
    for pass_index in range(PASSES):
        size_z = smoothed.shape[0] - 2
        size_x = smoothed.shape[1] - 2
        z0 = pass_index
        x0 = pass_index
        smoothed = tv_pass(
            smoothed,
            z_in[z0:z0 + size_z],
            z_in[z0 + 2:z0 + 2 + size_z],
            x_in[x0:x0 + size_x],
            x_in[x0 + 2:x0 + 2 + size_x],
        )
    sent = smoothed.astype(jnp.bfloat16)
    sent_pad = extended(sent, (("bz", 0), ("bxy", 1)), RADIUS)
    rows_pad = (cz_here + 2 * RADIUS) * (cx_here + 2 * RADIUS)
    rows = cz_here * cx_here
    sent_flat = sent_pad.astype(jnp.float32).reshape(rows_pad, cells_y)
    kernels = psf_taps / jnp.sum(psf_taps, axis=-1, keepdims=True)
    fwd_plane = plane_matrices(kernels[:, :, 0], kernels[:, :, 1], cz_here, cx_here)
    adj_plane = plane_matrices(kernels[:, :, 0, ::-1], kernels[:, :, 1, ::-1], cz_here, cx_here)
    lines = lax.optimization_barrier(line_matrices(kernels[:, :, 2], view_shift, cells_y))
    planes = jnp.einsum("vrqp,pj->vrqj", fwd_plane, sent_flat, precision=HIGH)
    images = jnp.einsum("vrqi,vrij->vqj", planes, lines, precision=HIGH) / RANK
    images = images.reshape(VIEWS, cz_here, cx_here, cells_y)
    flags = intersection[:, brick_z, brick_x]
    ratios = jnp.where(
        flags[:, None, None, None] > 0,
        observed.astype(jnp.float32) / (images + BACKGROUND),
        1.0,
    ).astype(jnp.bfloat16)
    ratio_pad = extended(ratios, (("bz", 1), ("bxy", 2)), RADIUS)
    ratio_flat = ratio_pad.astype(jnp.float32).reshape(VIEWS, rows_pad, cells_y)
    spread = jnp.einsum("vrqp,vpj->vrqj", adj_plane, ratio_flat, precision=HIGH)
    correction = jnp.einsum("vrqi,vrji->qj", spread, lines, precision=HIGH) / RANK
    correction = correction.reshape(cz_here, cx_here, cells_y)
    return smoothed * correction / VIEWS


def solution(mesh):
    return jax.shard_map(
        local,
        mesh=mesh,
        in_specs=(P("bz", "bxy", None), P(None, "bz", "bxy", None), P(), P(), P()),
        out_specs=P("bz", "bxy", None),
        check_vma=False,
    )
```

```python
import jax
import jax.numpy as jnp
from jax import lax
from jax.sharding import PartitionSpec as P

VIEWS = 3
RANK = 3
RADIUS = 4
PASSES = 8


EPS_TV = 0.25
TAU = 0.08
BACKGROUND = 0.1
HIGHEST = lax.Precision.HIGHEST
HIGH = lax.Precision.HIGH


def extended(cells, sides, width):
    for axis, dim in sides:
        count = lax.axis_size(axis)
        ends = count - 1
        head = lax.slice_in_dim(cells, 0, width, axis=dim)
        tail = lax.slice_in_dim(cells, cells.shape[dim] - width, cells.shape[dim], axis=dim)
        cells = jnp.concatenate(
            [
                lax.ppermute(tail, axis, [(i, (i + 1) % count) for i in range(ends)]),
                cells,
                lax.ppermute(head, axis, [((i + 1) % count, i) for i in range(ends)]),
            ],
            axis=dim,
        )
    return cells


def flux(diff):
    return diff / jnp.sqrt(diff * diff + EPS_TV)


def tv_pass(padded, z_lower, z_upper, x_lower, x_upper):
    field = padded[1:-1, 1:-1]
    cells_y = field.shape[2]
    along_j = lax.broadcasted_iota(jnp.int32, field.shape, 2)
    step_z = flux(padded[1:, 1:-1] - padded[:-1, 1:-1])
    step_x = flux(padded[1:-1, 1:] - padded[1:-1, :-1])
    step_y = flux(field[:, :, 1:] - field[:, :, :-1])
    pad_y = jnp.zeros(field.shape[:2] + (1,), field.dtype)
    up_y = jnp.concatenate([step_y, pad_y], axis=2)
    down_y = jnp.concatenate([pad_y, step_y], axis=2)
    total = jnp.zeros_like(field)
    total = total + -step_z[:-1] * z_lower[:, None, None]
    total = total + step_z[1:] * z_upper[:, None, None]
    total = total + -step_x[:, :-1] * x_lower[None, :, None]
    total = total + step_x[:, 1:] * x_upper[None, :, None]
    total = total + jnp.where(along_j >= 1, -down_y, 0.0)
    total = total + jnp.where(along_j < cells_y - 1, up_y, 0.0)
    return field + TAU * total


def band(taps, rows, cols):
    gap = lax.iota(jnp.int32, cols)[None, :] - lax.iota(jnp.int32, rows)[:, None]
    out = jnp.zeros(taps.shape[:-1] + (rows, cols), jnp.float32)
    for tap in range(taps.shape[-1]):
        out = out + jnp.where(gap == tap, taps[..., tap, None, None], 0.0)
    return out


def plane_matrices(kz, kx, cz, cx):
    wz = band(kz, cz, cz + 2 * RADIUS)
    wx = band(kx, cx, cx + 2 * RADIUS)
    wide = cx + 2 * RADIUS
    q = lax.iota(jnp.int32, cz * cx)
    p = lax.iota(jnp.int32, (cz + 2 * RADIUS) * wide)
    pick_qz = (q[:, None] // cx == lax.iota(jnp.int32, cz)[None, :]).astype(jnp.float32)
    pick_qx = (q[:, None] % cx == lax.iota(jnp.int32, cx)[None, :]).astype(jnp.float32)
    pick_pz = (lax.iota(jnp.int32, cz + 2 * RADIUS)[:, None] == p[None, :] // wide).astype(jnp.float32)
    pick_px = (lax.iota(jnp.int32, wide)[:, None] == p[None, :] % wide).astype(jnp.float32)
    full_z = jnp.einsum("qa,...ab,bp->...qp", pick_qz, wz, pick_pz, precision=HIGH)
    full_x = jnp.einsum("qa,...ab,bp->...qp", pick_qx, wx, pick_px, precision=HIGH)
    return full_z * full_x


def line_matrices(ky, shift, ny):
    rows = lax.iota(jnp.int32, ny)[None, :, None] + shift[:, None, None]
    rows = jnp.where(rows >= ny, rows - ny, rows)
    gap = rows - lax.iota(jnp.int32, ny)[None, None, :] + RADIUS
    gap = gap[:, None]
    out = jnp.zeros(ky.shape[:-1] + (ny, ny), jnp.float32)
    for tap in range(ky.shape[-1]):
        out = jnp.where(gap == tap, ky[..., tap, None, None], out)
    return out


def local(estimate, observed, psf_taps, view_shift, intersection):
    cz_here, cx_here, cells_y = estimate.shape
    bricks_z = lax.axis_size("bz")
    bricks_x = lax.axis_size("bxy")
    cells_z = cz_here * bricks_z
    cells_x = cx_here * bricks_x
    brick_z = lax.axis_index("bz")
    brick_x = lax.axis_index("bxy")
    z_base = brick_z * cz_here
    x_base = brick_x * cx_here
    smoothed = extended(estimate, (("bz", 0),), PASSES)
    smoothed, view_shift = lax.optimization_barrier((smoothed, view_shift))
    smoothed = extended(smoothed, (("bxy", 1),), PASSES)
    zc = z_base - PASSES + lax.iota(jnp.int32, smoothed.shape[0])
    xc = x_base - PASSES + lax.iota(jnp.int32, smoothed.shape[1])
    masks = lax.optimization_barrier((
        ((zc >= 0) & (zc < cells_z)).astype(jnp.float32),
        ((xc >= 0) & (xc < cells_x)).astype(jnp.float32),
    ))
    z_in, x_in = masks
    for pass_index in range(PASSES):
        size_z = smoothed.shape[0] - 2
        size_x = smoothed.shape[1] - 2
        z0 = pass_index
        x0 = pass_index
        smoothed = tv_pass(
            smoothed,
            z_in[z0:z0 + size_z],
            z_in[z0 + 2:z0 + 2 + size_z],
            x_in[x0:x0 + size_x],
            x_in[x0 + 2:x0 + 2 + size_x],
        )
    sent = smoothed.astype(jnp.bfloat16)
    sent_pad = extended(sent, (("bz", 0), ("bxy", 1)), RADIUS)
    rows_pad = (cz_here + 2 * RADIUS) * (cx_here + 2 * RADIUS)
    rows = cz_here * cx_here
    sent_flat = sent_pad.astype(jnp.float32).reshape(rows_pad, cells_y)
    kernels = psf_taps / jnp.sum(psf_taps, axis=-1, keepdims=True)
    fwd_plane = plane_matrices(kernels[:, :, 0], kernels[:, :, 1], cz_here, cx_here)
    adj_plane = plane_matrices(kernels[:, :, 0, ::-1], kernels[:, :, 1, ::-1], cz_here, cx_here)
    lines = lax.optimization_barrier(line_matrices(kernels[:, :, 2], view_shift, cells_y))
    planes = jnp.einsum("vrqp,pj->vrqj", fwd_plane, sent_flat, precision=HIGH)
    images = jnp.einsum("vrqi,vrij->vqj", planes, lines, precision=HIGH) / RANK
    images = images.reshape(VIEWS, cz_here, cx_here, cells_y)
    flags = intersection[:, brick_z, brick_x]
    ratios = jnp.where(
        flags[:, None, None, None] > 0,
        observed.astype(jnp.float32) / (images + BACKGROUND),
        1.0,
    ).astype(jnp.bfloat16)
    ratio_pad = extended(ratios, (("bz", 1), ("bxy", 2)), RADIUS)
    ratio_flat = ratio_pad.astype(jnp.float32).reshape(VIEWS, rows_pad, cells_y)
    spread = jnp.einsum("vrqp,vpj->vrqj", adj_plane, ratio_flat, precision=HIGH)
    correction = jnp.einsum("vrqi,vrji->qj", spread, lines, precision=HIGH) / RANK
    correction = correction.reshape(cz_here, cx_here, cells_y)
    return smoothed * correction / VIEWS


def solution(mesh):
    return jax.shard_map(
        local,
        mesh=mesh,
        in_specs=(P("bz", "bxy", None), P(None, "bz", "bxy", None), P(), P(), P()),
        out_specs=P("bz", "bxy", None),
        check_vma=False,
    )
```
